256 devices in a mesh: band: 16 (over y, z_lo), bin: 16 (over z_hi, x, core).
Axes of the slice: x: 4, y: 4, z: 8 (z_hi: 2, z_lo: 4; z = z_hi * 4 + z_lo), core: 2. Of those that a mesh axis runs over, the one named last changes fastest.
Arguments:
- spectrum: float32 [131072, 1152], P('band', 'bin'), may hold values from -6 to 6
- velocity: float32 [16384, 128], P(('band', 'bin')), may hold values from -5 to 5
- source_a: bfloat16 [1152, 1152], replicated, may hold values from -0.1875 to 0.1875
- source_b: bfloat16 [1152, 1152], replicated, may hold values from -0.1875 to 0.1875
- stokes_kernel: bfloat16 [1152, 128], replicated, may hold values from -0.1875 to 0.1875
- group_speed: float32 [1152], replicated, may hold values from 0.4 to 0.6
- column_map: int32 [131072], replicated, may hold values from 0 to 16383, as said below
- land_mask: int32 [131072], replicated, may hold values 0 or 1
Outputs:
- spectrum_out: float32 [131072, 1152], P('band', 'bin')
- velocity_out: float32 [16384, 128], P(('band', 'bin'))
The draws below stay inside these ranges and needn't reach their ends.
Inputs may be any that keep to these rules, and one draw needn't show every extreme that they name: `column_map`: the cells of the k-th aligned block of 512 cells belong to the 64 columns from k * 64 + 64 // 2 onward, counted modulo 16384, in rising order along the block; every column owns from 1 to 16 cells, and in every block some column owns exactly 16.
All inputs are finite; a program needn't handle non-finite values.
Results may differ from the reference program's by a relative error of at most 0.002.
Values may be sent and summed in bfloat16 or wider, within the bound.
No kernel may reach another device: no remote copies, remote signals or barrier semaphores. Data moves between devices by JAX's collectives and lax.ppermute only.
A program may use at most 64 MiB of HBM per device.

```python
import math
import jax
import jax.numpy as jnp
from jax import lax

NDIR = 36
LEVELS = 64
CELL_DEV = 512
CELLS_PER_COL = 8
STEPS = 2
BINS = 1152
COLS_DEV = 64
CELLS = 131072
OCOLS = 16384


def draw_column_map(key, part):
    blocks = CELLS // CELL_DEV
    pairs = COLS_DEV // 2
    key_shift, key_order = jax.random.split(key)
    moved = jax.random.randint(key_shift, (blocks, pairs), -(CELLS_PER_COL - 1), CELLS_PER_COL).astype(jnp.int32)
    lengths = jnp.stack([CELLS_PER_COL + moved, CELLS_PER_COL - moved], 2).reshape(blocks, COLS_DEV)
    planted = jnp.array([2 * CELLS_PER_COL, 1, CELLS_PER_COL - 1, CELLS_PER_COL], jnp.int32)
    lengths = lengths.at[:, :4].set(jnp.broadcast_to(planted[None, :], (blocks, 4)))
    block_keys = jax.random.split(key_order, blocks)
    orders = jax.vmap(lambda k: jax.random.permutation(k, COLS_DEV))(block_keys)
    lengths = jnp.take_along_axis(lengths, orders, 1)
    ends = jnp.cumsum(lengths, 1).astype(jnp.int32)
    position = jnp.arange(CELL_DEV, dtype=jnp.int32)
    local = jnp.sum((ends[:, None, :] <= position[None, :, None]).astype(jnp.int32), axis=2)
    block_ids = jnp.arange(blocks, dtype=jnp.int32)[:, None]
    column = (block_ids * COLS_DEV + COLS_DEV // 2 + local) % OCOLS
    return column.reshape(CELLS).astype(jnp.int32)


def place_ends(entries, own_key, low, largest):
    extent = entries.shape
    place = [jax.random.randint(jax.random.fold_in(own_key, axis), (), 0, extent[axis]) for axis in range(len(extent))]
    entries = entries.at[tuple(place)].set(low)
    longest = extent.index(max(extent))
    place[longest] = (place[longest] + 1) % extent[longest]
    return entries.at[tuple(place)].set(largest)


def levels(stream_key, dims, shards, least, top_value):
    factor_of = 1.0
    for dim, shards_of in shards:
        steps = jax.random.uniform(jax.random.fold_in(jax.random.fold_in(stream_key, 6), dim), (shards_of,), jnp.float32, least / len(shards), top_value / len(shards))
        factor_of = factor_of * jnp.repeat(jnp.exp(steps), dims[dim] // shards_of).reshape((-1,) + (1,) * (len(dims) - 1 - dim))
    return factor_of


def scatter_about(own_key, extent, scale, most, pieces=(), kind=jnp.bfloat16):
    values = jax.random.normal(own_key, extent, jnp.float32) * scale
    if len(pieces) > 0:
        values = levels(own_key, extent, pieces, -0.22, 0.18) * values
    return jnp.clip(values, min=-most, max=most).astype(kind)


def setup_inputs(seed: int = 0) -> dict:
    arg_keys = jax.random.split(jax.random.key(seed), 9)
    spectrum = scatter_about(arg_keys[0], (CELLS, BINS), 1.0, 6.0, ((0, 16), (1, 16)), jnp.float32)
    velocity = scatter_about(arg_keys[1], (OCOLS, 2 * LEVELS), 0.7, 5.0, ((0, 256),), jnp.float32)
    source_a = scatter_about(arg_keys[2], (BINS, BINS), BINS ** -0.5, 0.1875)
    source_b = scatter_about(arg_keys[3], (BINS, BINS), BINS ** -0.5, 0.1875)
    stokes_kernel = scatter_about(arg_keys[4], (BINS, 2 * LEVELS), BINS ** -0.5, 0.1875)
    group_speed = jnp.clip(jax.random.uniform(arg_keys[5], (BINS,), jnp.float32, 0.4, 0.6), 0.4, 0.6)
    column_map = draw_column_map(jax.random.fold_in(arg_keys[8], 71), 0)
    land_mask = place_ends((jax.random.randint(arg_keys[7], (CELLS,), 0, 8) < 7).astype(jnp.int32), jax.random.fold_in(arg_keys[7], 1), 0, 1)
    return dict(spectrum=spectrum, velocity=velocity, source_a=source_a, source_b=source_b, stokes_kernel=stokes_kernel, group_speed=group_speed, column_map=column_map, land_mask=land_mask)


def reference(spectrum, velocity, source_a, source_b, stokes_kernel, group_speed, column_map, land_mask):
    index = jnp.arange(BINS)
    angle = (2.0 * math.pi / NDIR) * (index % NDIR).astype(jnp.float32)
    cos_b = jnp.cos(angle)
    sin_b = jnp.sin(angle)
    mask = land_mask.astype(jnp.float32)
    counts = jax.ops.segment_sum(jnp.ones((CELLS,), jnp.float32), column_map, OCOLS)
    for step in range(STEPS):
        east = velocity[column_map, 0]
        north = velocity[column_map, LEVELS]
        speed = group_speed[None, :] + 0.25 * (jnp.tanh(east)[:, None] * cos_b[None, :] + jnp.tanh(north)[:, None] * sin_b[None, :])
        behind = jnp.concatenate([jnp.zeros((1, BINS), jnp.float32), spectrum[:-1]], 0)
        moved = mask[:, None] * (spectrum - speed * (spectrum - behind))
        rounded = moved.astype(jnp.bfloat16)

        def source_block(pair):
            rows, mrow = pair
            gain = jnp.dot(rows, source_a, preferred_element_type=jnp.float32)
            other = jnp.dot(rows, source_b, preferred_element_type=jnp.float32)
            increment = (0.1 * mrow[:, None] * (gain + 0.5 * gain * other)).astype(jnp.bfloat16)
            stokes = jnp.dot(rows, stokes_kernel, preferred_element_type=jnp.float32)
            return increment, stokes

        increment, stokes = lax.map(source_block, (rounded.reshape(-1, CELL_DEV, BINS), mask.reshape(-1, CELL_DEV)))
        spectrum = moved + increment.reshape(CELLS, BINS).astype(jnp.float32)
        forcing = jax.ops.segment_sum(stokes.reshape(CELLS, 2 * LEVELS), column_map, OCOLS) / counts[:, None]
        padded = jnp.pad(velocity, ((1, 1), (0, 0)))
        lap_h = padded[2:] + padded[:-2] - 2.0 * velocity
        cube = velocity.reshape(OCOLS, 2, LEVELS)
        edge = jnp.pad(cube, ((0, 0), (0, 0), (1, 1)), mode="edge")
        lap_v = (edge[:, :, 2:] + edge[:, :, :-2] - 2.0 * cube).reshape(OCOLS, 2 * LEVELS)
        velocity = velocity + 0.2 * lap_h + 0.2 * lap_v + 1.5 * forcing - 0.05 * velocity
    return spectrum, velocity
```

```python
import math

import jax
import jax.numpy as jnp
from jax import lax
from jax.sharding import PartitionSpec as P

NDIR = 36
LEVELS = 64
STEPS = 2
ALL = ("band", "bin")


def shifted(block, axis, distance):
    devices = range(lax.axis_size(axis))
    route = [((i - distance) % len(devices), i) for i in devices]
    return lax.ppermute(block, axis, route)


def from_behind(shard, axis, by):
    peers = lax.axis_size(axis)
    pairs = [(i, i + by) for i in range(peers) if 0 <= i + by < peers]
    return lax.ppermute(shard, axis, pairs)


def bin_angles(count):
    index = jnp.arange(count)
    angle = 2.0 * math.pi / NDIR * (index % NDIR).astype(jnp.float32)
    return (jnp.cos(angle), jnp.sin(angle))


def propagate(field, prev, current, speed_bins, cos_b, sin_b, mask_cells):
    speed = speed_bins[None, :] + 0.25 * (
        jnp.tanh(current[0])[:, None] * cos_b[None, :]
        + jnp.tanh(current[1])[:, None] * sin_b[None, :]
    )
    behind = jnp.concatenate([prev, field[:-1]], 0)
    return mask_cells[:, None] * (field - speed * (field - behind))


def sources(rounded, mask_cells, source_a, source_b, stokes_kernel):
    gain = jnp.dot(rounded, source_a, preferred_element_type=jnp.float32)
    other = jnp.dot(rounded, source_b, preferred_element_type=jnp.float32)
    increment = (0.1 * mask_cells[:, None] * (gain + 0.5 * gain * other)).astype(jnp.bfloat16)
    stokes = jnp.dot(rounded, stokes_kernel, preferred_element_type=jnp.float32)
    return (increment, stokes)


def ocean_step(window, below, above, forcing, joint):
    columns = window.shape[0]
    padded = jnp.concatenate([below, window, above], 0)
    up = padded[2:]
    down = padded[:-2]
    if joint is not None:
        row = jnp.arange(columns)[:, None]
        up = jnp.where(joint & (row == columns // 2 - 1), 0.0, up)
        down = jnp.where(joint & (row == columns // 2), 0.0, down)
    lap_h = up + down - 2.0 * window
    cube = window.reshape(columns, 2, LEVELS)
    edge = jnp.pad(cube, ((0, 0), (0, 0), (1, 1)), mode="edge")
    lap_v = (edge[:, :, 2:] + edge[:, :, :-2] - 2.0 * cube).reshape(columns, 2 * LEVELS)
    return window + 0.2 * lap_h + 0.2 * lap_v + 1.5 * forcing - 0.05 * window


def per_device(
    spectrum, velocity, source_a, source_b, stokes_kernel, group_speed, column_map, land_mask
):
    bin_count = lax.axis_size("bin")
    device_count = lax.axis_size("band") * bin_count
    device = lax.axis_index("band") * bin_count + lax.axis_index("bin")
    cell_dev = spectrum.shape[0] // bin_count
    columns = velocity.shape[0]
    half = columns // 2
    total = columns * device_count
    bins = spectrum.shape[1] * bin_count

    cell_first = device * cell_dev
    local_map = lax.dynamic_slice_in_dim(column_map, cell_first, cell_dev)
    local_mask = lax.dynamic_slice_in_dim(land_mask, cell_first, cell_dev).astype(jnp.float32)
    cos_b, sin_b = bin_angles(bins)

    first = device * columns + half
    where = jnp.mod(local_map - first, total)
    onehot = (where[None, :] == jnp.arange(columns)[:, None]).astype(jnp.float32)
    counts = jnp.sum(onehot, axis=1)
    joint = (device == device_count - 1) if device_count > 1 else None

    upper = shifted(velocity[: half + 1], ALL, -1)
    window = jnp.concatenate([velocity[half:], upper[:half]], 0)
    below = velocity[half - 1 : half]
    above = upper[half:]

    field = lax.all_to_all(spectrum, "bin", split_axis=0, concat_axis=1, tiled=True)
    for step in range(STEPS):
        current = jnp.stack(
            [jnp.take(window[:, 0], where, axis=0), jnp.take(window[:, LEVELS], where, axis=0)]
        )
        prev = from_behind(field[-1:], ALL, 1)
        moved = propagate(field, prev, current, group_speed, cos_b, sin_b, local_mask)
        increment, stokes = sources(
            moved.astype(jnp.bfloat16), local_mask, source_a, source_b, stokes_kernel
        )
        field = moved + increment.astype(jnp.float32)
        sums = jnp.dot(onehot, stokes, precision=lax.Precision.HIGHEST)
        forcing = sums / counts[:, None]
        if step > 0:
            below = shifted(window[-1:], ALL, 1)
            above = shifted(window[:1], ALL, -1)
        window = ocean_step(window, below, above, forcing, joint)
    velocity_out = jnp.concatenate([shifted(window[half:], ALL, 1), window[:half]], 0)
    spectrum_out = lax.all_to_all(field, "bin", split_axis=1, concat_axis=0, tiled=True)
    return (spectrum_out, velocity_out)


def solution(mesh):
    in_specs = (P("band", "bin"), P(ALL, None), P(), P(), P(), P(), P(), P())
    out_specs = (P("band", "bin"), P(ALL, None))
    return jax.shard_map(
        per_device, mesh=mesh, in_specs=in_specs, out_specs=out_specs, check_vma=False
    )
```

```python
import math

import jax
import jax.numpy as jnp
from jax import lax
from jax.sharding import PartitionSpec as P

NDIR = 36
LEVELS = 64
STEPS = 2
ALL = ("band", "bin")
EXTRA = 8


def shifted(block, axis, distance):
    devices = range(lax.axis_size(axis))
    route = [((i - distance) % len(devices), i) for i in devices]
    return lax.ppermute(block, axis, route)


def from_behind(shard, axis, by):
    peers = lax.axis_size(axis)
    pairs = [(i, i + by) for i in range(peers) if 0 <= i + by < peers]
    return lax.ppermute(shard, axis, pairs)


def bin_angles(count):
    index = jnp.arange(count)
    angle = 2.0 * math.pi / NDIR * (index % NDIR).astype(jnp.float32)
    return (jnp.cos(angle), jnp.sin(angle))


def propagate(field, prev, current, speed_bins, cos_b, sin_b, mask_cells):
    speed = speed_bins[None, :] + 0.25 * (
        jnp.tanh(current[0])[:, None] * cos_b[None, :]
        + jnp.tanh(current[1])[:, None] * sin_b[None, :]
    )
    behind = jnp.concatenate([prev, field[:-1]], 0)
    return mask_cells[:, None] * (field - speed * (field - behind))


def sources(rounded, mask_cells, source_a, source_b, stokes_kernel):
    gain = jnp.dot(rounded, source_a, preferred_element_type=jnp.float32)
    other = jnp.dot(rounded, source_b, preferred_element_type=jnp.float32)
    increment = (0.1 * mask_cells[:, None] * (gain + 0.5 * gain * other)).astype(jnp.bfloat16)
    stokes = jnp.dot(rounded, stokes_kernel, preferred_element_type=jnp.float32)
    return (increment, stokes)


def ocean_step(window, below, above, forcing, joint):
    columns = window.shape[0]
    padded = jnp.concatenate([below, window, above], 0)
    up = padded[2:]
    down = padded[:-2]
    if joint is not None:
        row = jnp.arange(columns)[:, None]
        up = jnp.where(joint & (row == columns // 2 - 1), 0.0, up)
        down = jnp.where(joint & (row == columns // 2), 0.0, down)
    lap_h = up + down - 2.0 * window
    cube = window.reshape(columns, 2, LEVELS)
    edge = jnp.pad(cube, ((0, 0), (0, 0), (1, 1)), mode="edge")
    lap_v = (edge[:, :, 2:] + edge[:, :, :-2] - 2.0 * cube).reshape(columns, 2 * LEVELS)
    return window + 0.2 * lap_h + 0.2 * lap_v + 1.5 * forcing - 0.05 * window


def per_device(
    spectrum, velocity, source_a, source_b, stokes_kernel, group_speed, column_map, land_mask
):
    bin_count = lax.axis_size("bin")
    device_count = lax.axis_size("band") * bin_count
    device = lax.axis_index("band") * bin_count + lax.axis_index("bin")
    cell_dev = spectrum.shape[0] // bin_count
    columns = velocity.shape[0]
    half = columns // 2
    total = columns * device_count
    bins = spectrum.shape[1] * bin_count

    cell_first = device * cell_dev
    ext_map = lax.dynamic_slice_in_dim(
        jnp.concatenate([column_map[-EXTRA:], column_map]), cell_first, cell_dev + EXTRA
    )
    ext_mask = lax.dynamic_slice_in_dim(
        jnp.concatenate([land_mask[-EXTRA:], land_mask]), cell_first, cell_dev + EXTRA
    ).astype(jnp.float32)
    local_map = ext_map[EXTRA:]
    local_mask = ext_mask[EXTRA:]
    cos_b, sin_b = bin_angles(bins)

    first = device * columns + half
    where = jnp.mod(local_map - first, total)
    onehot = (where[None, :] == jnp.arange(columns)[:, None]).astype(jnp.float32)
    counts = jnp.sum(onehot, axis=1)
    joint = (device == device_count - 1) if device_count > 1 else None

    upper = shifted(velocity[: half + 1], ALL, -1)
    window = jnp.concatenate([velocity[half:], upper[:half]], 0)
    below = velocity[half - 1 : half]
    above = upper[half:]

    own = jnp.concatenate([velocity, upper[:half]], 0)
    ext_where = jnp.mod(ext_map - device * columns, total)
    table = jnp.stack([own[:, 0], own[:, LEVELS]])
    current = jnp.take(table, ext_where, axis=1)

    tail = from_behind(spectrum[-EXTRA:], "band", 1)
    blocks = spectrum.reshape(bin_count, cell_dev, spectrum.shape[1])
    heads = jnp.concatenate([tail[None], blocks[:-1, -EXTRA:]], 0)
    sent = jnp.concatenate([heads, blocks], 1).reshape(-1, spectrum.shape[1])
    field = lax.all_to_all(sent, "bin", split_axis=0, concat_axis=1, tiled=True)
    prev = jnp.zeros((1, bins), jnp.float32)
    mask = ext_mask
    for step in range(STEPS):
        moved = propagate(field, prev, current, group_speed, cos_b, sin_b, mask)
        increment, stokes = sources(
            moved.astype(jnp.bfloat16), mask, source_a, source_b, stokes_kernel
        )
        field = moved + increment.astype(jnp.float32)
        if step == 0:
            prev = field[EXTRA - 1 : EXTRA]
            field = field[EXTRA:]
            stokes = stokes[EXTRA:]
            mask = local_mask
        sums = jnp.dot(onehot, stokes, precision=lax.Precision.HIGHEST)
        forcing = sums / counts[:, None]
        if step > 0:
            below = shifted(window[-1:], ALL, 1)
            above = shifted(window[:1], ALL, -1)
        window = ocean_step(window, below, above, forcing, joint)
        if step + 1 < STEPS:
            table = jnp.stack([window[:, 0], window[:, LEVELS]])
            current = jnp.take(table, where, axis=1)
    velocity_out = jnp.concatenate([shifted(window[half:], ALL, 1), window[:half]], 0)
    spectrum_out = lax.all_to_all(field, "bin", split_axis=1, concat_axis=0, tiled=True)
    return (spectrum_out, velocity_out)


def solution(mesh):
    in_specs = (P("band", "bin"), P(ALL, None), P(), P(), P(), P(), P(), P())
    out_specs = (P("band", "bin"), P(ALL, None))
    return jax.shard_map(
        per_device, mesh=mesh, in_specs=in_specs, out_specs=out_specs, check_vma=False
    )
```

```python
import math

import jax
import jax.numpy as jnp
from jax import lax
from jax.sharding import PartitionSpec as P

NDIR = 36
LEVELS = 64
STEPS = 2
ALL = ("band", "bin")
EXTRA = 8


def shifted(block, axis, distance):
    devices = range(lax.axis_size(axis))
    route = [((i - distance) % len(devices), i) for i in devices]
    return lax.ppermute(block, axis, route)


def from_behind(shard, axis, by):
    peers = lax.axis_size(axis)
    pairs = [(i, i + by) for i in range(peers) if 0 <= i + by < peers]
    return lax.ppermute(shard, axis, pairs)


def bin_angles(count):
    index = jnp.arange(count)
    angle = 2.0 * math.pi / NDIR * (index % NDIR).astype(jnp.float32)
    return (jnp.cos(angle), jnp.sin(angle))


def propagate(field, prev, current, speed_bins, cos_b, sin_b, mask_cells):
    speed = speed_bins[None, :] + 0.25 * (
        jnp.tanh(current[0])[:, None] * cos_b[None, :]
        + jnp.tanh(current[1])[:, None] * sin_b[None, :]
    )
    behind = jnp.concatenate([prev, field[:-1]], 0)
    return mask_cells[:, None] * (field - speed * (field - behind))


def sources(rounded, mask_cells, source_a, source_b, stokes_kernel):
    gain = jnp.dot(rounded, source_a, preferred_element_type=jnp.float32)
    other = jnp.dot(rounded, source_b, preferred_element_type=jnp.float32)
    increment = (0.1 * mask_cells[:, None] * (gain + 0.5 * gain * other)).astype(jnp.bfloat16)
    stokes = jnp.dot(rounded, stokes_kernel, preferred_element_type=jnp.float32)
    return (increment, stokes)


def ocean_step(window, below, above, forcing, joint):
    columns = window.shape[0]
    padded = jnp.concatenate([below, window, above], 0)
    up = padded[2:]
    down = padded[:-2]
    if joint is not None:
        row = jnp.arange(columns)[:, None]
        up = jnp.where(joint & (row == columns // 2 - 1), 0.0, up)
        down = jnp.where(joint & (row == columns // 2), 0.0, down)
    lap_h = up + down - 2.0 * window
    cube = window.reshape(columns, 2, LEVELS)
    edge = jnp.pad(cube, ((0, 0), (0, 0), (1, 1)), mode="edge")
    lap_v = (edge[:, :, 2:] + edge[:, :, :-2] - 2.0 * cube).reshape(columns, 2 * LEVELS)
    return window + 0.2 * lap_h + 0.2 * lap_v + 1.5 * forcing - 0.05 * window


def per_device(
    spectrum, velocity, source_a, source_b, stokes_kernel, group_speed, column_map, land_mask
):
    bin_count = lax.axis_size("bin")
    device_count = lax.axis_size("band") * bin_count
    device = lax.axis_index("band") * bin_count + lax.axis_index("bin")
    cell_dev = spectrum.shape[0] // bin_count
    columns = velocity.shape[0]
    half = columns // 2
    total = columns * device_count
    bins = spectrum.shape[1] * bin_count

    cell_first = device * cell_dev
    ext_map = lax.dynamic_slice_in_dim(
        jnp.concatenate([column_map[-EXTRA:], column_map]), cell_first, cell_dev + EXTRA
    )
    ext_mask = lax.dynamic_slice_in_dim(
        jnp.concatenate([land_mask[-EXTRA:], land_mask]), cell_first, cell_dev + EXTRA
    ).astype(jnp.float32)
    local_map = ext_map[EXTRA:]
    local_mask = ext_mask[EXTRA:]
    cos_b, sin_b = bin_angles(bins)

    first = device * columns + half
    where = jnp.mod(local_map - first, total)
    onehot = (where[None, :] == jnp.arange(columns)[:, None]).astype(jnp.float32)
    counts = jnp.sum(onehot, axis=1)
    joint = (device == device_count - 1) if device_count > 1 else None

    upper = shifted(velocity[: half + 1], ALL, -1)
    window = jnp.concatenate([velocity[half:], upper[:half]], 0)
    below = velocity[half - 1 : half]
    above = upper[half:]

    own = jnp.concatenate([velocity, upper[:half]], 0)
    ext_where = jnp.mod(ext_map - device * columns, total)
    table = jnp.stack([own[:, 0], own[:, LEVELS]])
    current = jnp.take(table, ext_where, axis=1)

    tail = from_behind(spectrum[-EXTRA:], "band", 1)
    blocks = spectrum.reshape(bin_count, cell_dev, spectrum.shape[1])
    heads = jnp.concatenate([tail[None], blocks[:-1, -EXTRA:]], 0).reshape(-1, spectrum.shape[1])
    body = lax.all_to_all(spectrum, "bin", split_axis=0, concat_axis=1, tiled=True)
    head = lax.all_to_all(heads, "bin", split_axis=0, concat_axis=1, tiled=True)
    field = jnp.concatenate([head, body], 0)
    prev = jnp.zeros((1, bins), jnp.float32)
    mask = ext_mask
    for step in range(STEPS):
        moved = propagate(field, prev, current, group_speed, cos_b, sin_b, mask)
        increment, stokes = sources(
            moved.astype(jnp.bfloat16), mask, source_a, source_b, stokes_kernel
        )
        field = moved + increment.astype(jnp.float32)
        if step == 0:
            prev = field[EXTRA - 1 : EXTRA]
            field = field[EXTRA:]
            stokes = stokes[EXTRA:]
            mask = local_mask
        sums = jnp.dot(onehot, stokes, precision=lax.Precision.HIGHEST)
        forcing = sums / counts[:, None]
        if step > 0:
            below = shifted(window[-1:], ALL, 1)
            above = shifted(window[:1], ALL, -1)
        window = ocean_step(window, below, above, forcing, joint)
        if step + 1 < STEPS:
            table = jnp.stack([window[:, 0], window[:, LEVELS]])
            current = jnp.take(table, where, axis=1)
    velocity_out = jnp.concatenate([shifted(window[half:], ALL, 1), window[:half]], 0)
    spectrum_out = lax.all_to_all(field, "bin", split_axis=1, concat_axis=0, tiled=True)
    return (spectrum_out, velocity_out)


def solution(mesh):
    in_specs = (P("band", "bin"), P(ALL, None), P(), P(), P(), P(), P(), P())
    out_specs = (P("band", "bin"), P(ALL, None))
    return jax.shard_map(
        per_device, mesh=mesh, in_specs=in_specs, out_specs=out_specs, check_vma=False
    )
```

```python
import math

import jax
import jax.numpy as jnp
from jax import lax
from jax.sharding import PartitionSpec as P

NDIR = 36
LEVELS = 64
STEPS = 2
ALL = ("band", "bin")
EXTRA = 8


def shifted(block, axis, distance):
    devices = range(lax.axis_size(axis))
    route = [((i - distance) % len(devices), i) for i in devices]
    return lax.ppermute(block, axis, route)


def from_behind(shard, axis, by):
    peers = lax.axis_size(axis)
    pairs = [(i, i + by) for i in range(peers) if 0 <= i + by < peers]
    return lax.ppermute(shard, axis, pairs)


def bin_angles(count):
    index = jnp.arange(count)
    angle = 2.0 * math.pi / NDIR * (index % NDIR).astype(jnp.float32)
    return (jnp.cos(angle), jnp.sin(angle))


def propagate(field, prev, current, speed_bins, cos_b, sin_b, mask_cells):
    speed = speed_bins[None, :] + 0.25 * (
        jnp.tanh(current[0])[:, None] * cos_b[None, :]
        + jnp.tanh(current[1])[:, None] * sin_b[None, :]
    )
    behind = jnp.concatenate([prev, field[:-1]], 0)
    return mask_cells[:, None] * (field - speed * (field - behind))


def sources(rounded, mask_cells, source_a, source_b, stokes_kernel):
    gain = jnp.dot(rounded, source_a, preferred_element_type=jnp.float32)
    other = jnp.dot(rounded, source_b, preferred_element_type=jnp.float32)
    increment = (0.1 * mask_cells[:, None] * (gain + 0.5 * gain * other)).astype(jnp.bfloat16)
    stokes = jnp.dot(rounded, stokes_kernel, preferred_element_type=jnp.float32)
    return (increment, stokes)


def ocean_step(window, below, above, forcing, joint):
    columns = window.shape[0]
    padded = jnp.concatenate([below, window, above], 0)
    up = padded[2:]
    down = padded[:-2]
    if joint is not None:
        row = jnp.arange(columns)[:, None]
        up = jnp.where(joint & (row == columns // 2 - 1), 0.0, up)
        down = jnp.where(joint & (row == columns // 2), 0.0, down)
    lap_h = up + down - 2.0 * window
    cube = window.reshape(columns, 2, LEVELS)
    edge = jnp.pad(cube, ((0, 0), (0, 0), (1, 1)), mode="edge")
    lap_v = (edge[:, :, 2:] + edge[:, :, :-2] - 2.0 * cube).reshape(columns, 2 * LEVELS)
    return window + 0.2 * lap_h + 0.2 * lap_v + 1.5 * forcing - 0.05 * window


def per_device(
    spectrum, velocity, source_a, source_b, stokes_kernel, group_speed, column_map, land_mask
):
    bin_count = lax.axis_size("bin")
    device_count = lax.axis_size("band") * bin_count
    device = lax.axis_index("band") * bin_count + lax.axis_index("bin")
    cell_dev = spectrum.shape[0] // bin_count
    columns = velocity.shape[0]
    half = columns // 2
    total = columns * device_count
    bins = spectrum.shape[1] * bin_count

    cell_first = device * cell_dev
    ext_map = lax.dynamic_slice_in_dim(
        jnp.concatenate([column_map[-EXTRA:], column_map]), cell_first, cell_dev + EXTRA
    )
    ext_mask = lax.dynamic_slice_in_dim(
        jnp.concatenate([land_mask[-EXTRA:], land_mask]), cell_first, cell_dev + EXTRA
    ).astype(jnp.float32)
    local_map = ext_map[EXTRA:]
    local_mask = ext_mask[EXTRA:]
    cos_b, sin_b = bin_angles(bins)

    first = device * columns + half
    where = jnp.mod(local_map - first, total)
    onehot = (where[None, :] == jnp.arange(columns)[:, None]).astype(jnp.float32)
    counts = jnp.sum(onehot, axis=1)
    joint = (device == device_count - 1) if device_count > 1 else None

    upper = shifted(velocity[: half + 1], ALL, -1)
    window = jnp.concatenate([velocity[half:], upper[:half]], 0)
    below = velocity[half - 1 : half]
    above = upper[half:]

    own = jnp.concatenate([velocity, upper[:half]], 0)
    ext_where = jnp.mod(ext_map - device * columns, total)
    table = jnp.stack([own[:, 0], own[:, LEVELS]])
    current = jnp.take(table, ext_where, axis=1)

    width = spectrum.shape[1]
    tail = from_behind(spectrum[-2:], "band", 1)
    before = [tail] + [spectrum[j * cell_dev - 2 : j * cell_dev] for j in range(1, bin_count)]
    heads = jnp.stack([h[::-1] for h in before]).reshape(bin_count, 2 * width)
    heads = jnp.pad(heads, ((0, 0), (0, cell_dev - 2 * width)))
    slab = jnp.pad(heads[:, :, None], ((0, 0), (0, 0), (0, 7)))
    sent = jnp.concatenate([spectrum.reshape(bin_count, cell_dev, width), slab], 2)
    got = lax.all_to_all(sent, "bin", split_axis=0, concat_axis=0, tiled=True)
    body = got[:, :, :width].transpose(1, 0, 2).reshape(cell_dev, bins)
    head = got[:, : 2 * width, width].reshape(bin_count, 2, width).transpose(1, 0, 2)
    head = head.reshape(2, bins)[::-1]
    field = jnp.concatenate([jnp.zeros((EXTRA - 2, bins), jnp.float32), head, body], 0)
    prev = jnp.zeros((1, bins), jnp.float32)
    mask = ext_mask
    for step in range(STEPS):
        moved = propagate(field, prev, current, group_speed, cos_b, sin_b, mask)
        increment, stokes = sources(
            moved.astype(jnp.bfloat16), mask, source_a, source_b, stokes_kernel
        )
        field = moved + increment.astype(jnp.float32)
        if step == 0:
            prev = field[EXTRA - 1 : EXTRA]
            field = field[EXTRA:]
            stokes = stokes[EXTRA:]
            mask = local_mask
        sums = jnp.dot(onehot, stokes, precision=lax.Precision.HIGHEST)
        forcing = sums / counts[:, None]
        if step > 0:
            below = shifted(window[-1:], ALL, 1)
            above = shifted(window[:1], ALL, -1)
        window = ocean_step(window, below, above, forcing, joint)
        if step + 1 < STEPS:
            table = jnp.stack([window[:, 0], window[:, LEVELS]])
            current = jnp.take(table, where, axis=1)
    velocity_out = jnp.concatenate([shifted(window[half:], ALL, 1), window[:half]], 0)
    spectrum_out = lax.all_to_all(field, "bin", split_axis=1, concat_axis=0, tiled=True)
    return (spectrum_out, velocity_out)


def solution(mesh):
    in_specs = (P("band", "bin"), P(ALL, None), P(), P(), P(), P(), P(), P())
    out_specs = (P("band", "bin"), P(ALL, None))
    return jax.shard_map(
        per_device, mesh=mesh, in_specs=in_specs, out_specs=out_specs, check_vma=False
    )
```

```python
import math

import jax
import jax.numpy as jnp
from jax import lax
from jax.sharding import PartitionSpec as P

NDIR = 36
LEVELS = 64
STEPS = 2
ALL = ("band", "bin")
EXTRA = 8


def shifted(block, axis, distance):
    devices = range(lax.axis_size(axis))
    route = [((i - distance) % len(devices), i) for i in devices]
    return lax.ppermute(block, axis, route)


def from_behind(shard, axis, by):
    peers = lax.axis_size(axis)
    pairs = [(i, i + by) for i in range(peers) if 0 <= i + by < peers]
    return lax.ppermute(shard, axis, pairs)


def bin_angles(count):
    index = jnp.arange(count)
    angle = 2.0 * math.pi / NDIR * (index % NDIR).astype(jnp.float32)
    return (jnp.cos(angle), jnp.sin(angle))


def propagate(field, prev, current, speed_bins, cos_b, sin_b, mask_cells):
    speed = speed_bins[None, :] + 0.25 * (
        jnp.tanh(current[0])[:, None] * cos_b[None, :]
        + jnp.tanh(current[1])[:, None] * sin_b[None, :]
    )
    behind = jnp.concatenate([prev, field[:-1]], 0)
    return mask_cells[:, None] * (field - speed * (field - behind))


def sources(rounded, mask_cells, source_a, source_b, stokes_kernel):
    gain = jnp.dot(rounded, source_a, preferred_element_type=jnp.float32)
    other = jnp.dot(rounded, source_b, preferred_element_type=jnp.float32)
    increment = (0.1 * mask_cells[:, None] * (gain + 0.5 * gain * other)).astype(jnp.bfloat16)
    stokes = jnp.dot(rounded, stokes_kernel, preferred_element_type=jnp.float32)
    return (increment, stokes)


def ocean_step(window, below, above, forcing, joint):
    columns = window.shape[0]
    padded = jnp.concatenate([below, window, above], 0)
    up = padded[2:]
    down = padded[:-2]
    if joint is not None:
        row = jnp.arange(columns)[:, None]
        up = jnp.where(joint & (row == columns // 2 - 1), 0.0, up)
        down = jnp.where(joint & (row == columns // 2), 0.0, down)
    lap_h = up + down - 2.0 * window
    cube = window.reshape(columns, 2, LEVELS)
    edge = jnp.pad(cube, ((0, 0), (0, 0), (1, 1)), mode="edge")
    lap_v = (edge[:, :, 2:] + edge[:, :, :-2] - 2.0 * cube).reshape(columns, 2 * LEVELS)
    return window + 0.2 * lap_h + 0.2 * lap_v + 1.5 * forcing - 0.05 * window


def per_device(
    spectrum, velocity, source_a, source_b, stokes_kernel, group_speed, column_map, land_mask
):
    bin_count = lax.axis_size("bin")
    device_count = lax.axis_size("band") * bin_count
    device = lax.axis_index("band") * bin_count + lax.axis_index("bin")
    cell_dev = spectrum.shape[0] // bin_count
    columns = velocity.shape[0]
    half = columns // 2
    total = columns * device_count
    bins = spectrum.shape[1] * bin_count

    cell_first = device * cell_dev
    ext_map = lax.dynamic_slice_in_dim(
        jnp.concatenate([column_map[-EXTRA:], column_map]), cell_first, cell_dev + EXTRA
    )
    ext_mask = lax.dynamic_slice_in_dim(
        jnp.concatenate([land_mask[-EXTRA:], land_mask]), cell_first, cell_dev + EXTRA
    ).astype(jnp.float32)
    local_map = ext_map[EXTRA:]
    local_mask = ext_mask[EXTRA:]
    cos_b, sin_b = bin_angles(bins)

    first = device * columns + half
    where = jnp.mod(local_map - first, total)
    onehot = (where[None, :] == jnp.arange(columns)[:, None]).astype(jnp.float32)
    counts = jnp.sum(onehot, axis=1)
    joint = (device == device_count - 1) if device_count > 1 else None

    upper = shifted(velocity[: half + 1], ALL, -1)
    window = jnp.concatenate([velocity[half:], upper[:half]], 0)
    below = velocity[half - 1 : half]
    above = upper[half:]

    own = jnp.concatenate([velocity, upper[:half]], 0)
    ext_where = jnp.mod(ext_map - device * columns, total)
    table = jnp.stack([own[:, 0], own[:, LEVELS]])
    current = jnp.take(table, ext_where, axis=1)

    width = spectrum.shape[1]
    across = spectrum.T.reshape(width, bin_count, cell_dev)
    tail = from_behind(spectrum.T[:, -EXTRA:], "band", 1)
    before = jnp.concatenate([tail[:, None], across[:, :-1, -EXTRA:]], 1)
    slab = jnp.pad(before.transpose(1, 2, 0), ((0, 0), (0, 0), (0, cell_dev - width)))
    sent = jnp.concatenate([across.transpose(1, 0, 2), slab], 1)
    got = lax.all_to_all(sent, "bin", split_axis=0, concat_axis=0, tiled=True)
    body = got[:, :width, :].transpose(2, 0, 1).reshape(cell_dev, bins)
    head = got[:, width:, :width].transpose(1, 0, 2).reshape(EXTRA, bins)
    field = jnp.concatenate([head, body], 0)
    prev = jnp.zeros((1, bins), jnp.float32)
    mask = ext_mask
    for step in range(STEPS):
        moved = propagate(field, prev, current, group_speed, cos_b, sin_b, mask)
        increment, stokes = sources(
            moved.astype(jnp.bfloat16), mask, source_a, source_b, stokes_kernel
        )
        field = moved + increment.astype(jnp.float32)
        if step == 0:
            prev = field[EXTRA - 1 : EXTRA]
            field = field[EXTRA:]
            stokes = stokes[EXTRA:]
            mask = local_mask
        sums = jnp.dot(onehot, stokes, precision=lax.Precision.HIGHEST)
        forcing = sums / counts[:, None]
        if step > 0:
            below = shifted(window[-1:], ALL, 1)
            above = shifted(window[:1], ALL, -1)
        window = ocean_step(window, below, above, forcing, joint)
        if step + 1 < STEPS:
            table = jnp.stack([window[:, 0], window[:, LEVELS]])
            current = jnp.take(table, where, axis=1)
    velocity_out = jnp.concatenate([shifted(window[half:], ALL, 1), window[:half]], 0)
    spectrum_out = lax.all_to_all(field, "bin", split_axis=1, concat_axis=0, tiled=True)
    return (spectrum_out, velocity_out)


def solution(mesh):
    in_specs = (P("band", "bin"), P(ALL, None), P(), P(), P(), P(), P(), P())
    out_specs = (P("band", "bin"), P(ALL, None))
    return jax.shard_map(
        per_device, mesh=mesh, in_specs=in_specs, out_specs=out_specs, check_vma=False
    )
```

```python
import math

import jax
import jax.numpy as jnp
from jax import lax
from jax.sharding import PartitionSpec as P

NDIR = 36
LEVELS = 64
STEPS = 2
ALL = ("band", "bin")
EXTRA = 8


def shifted(block, axis, distance):
    devices = range(lax.axis_size(axis))
    route = [((i - distance) % len(devices), i) for i in devices]
    return lax.ppermute(block, axis, route)


def from_behind(shard, axis, by):
    peers = lax.axis_size(axis)
    pairs = [(i, i + by) for i in range(peers) if 0 <= i + by < peers]
    return lax.ppermute(shard, axis, pairs)


def bin_angles(count):
    index = jnp.arange(count)
    angle = 2.0 * math.pi / NDIR * (index % NDIR).astype(jnp.float32)
    return (jnp.cos(angle), jnp.sin(angle))


def propagate(field, prev, current, speed_bins, cos_b, sin_b, mask_cells):
    speed = speed_bins[None, :] + 0.25 * (
        jnp.tanh(current[0])[:, None] * cos_b[None, :]
        + jnp.tanh(current[1])[:, None] * sin_b[None, :]
    )
    behind = jnp.concatenate([prev, field[:-1]], 0)
    return mask_cells[:, None] * (field - speed * (field - behind))


def sources(rounded, mask_cells, source_a, source_b, stokes_kernel):
    gain = jnp.dot(rounded, source_a, preferred_element_type=jnp.float32)
    other = jnp.dot(rounded, source_b, preferred_element_type=jnp.float32)
    increment = (0.1 * mask_cells[:, None] * (gain + 0.5 * gain * other)).astype(jnp.bfloat16)
    stokes = jnp.dot(rounded, stokes_kernel, preferred_element_type=jnp.float32)
    return (increment, stokes)


def ocean_step(window, below, above, forcing, joint):
    columns = window.shape[0]
    padded = jnp.concatenate([below, window, above], 0)
    up = padded[2:]
    down = padded[:-2]
    if joint is not None:
        row = jnp.arange(columns)[:, None]
        up = jnp.where(joint & (row == columns // 2 - 1), 0.0, up)
        down = jnp.where(joint & (row == columns // 2), 0.0, down)
    lap_h = up + down - 2.0 * window
    cube = window.reshape(columns, 2, LEVELS)
    edge = jnp.pad(cube, ((0, 0), (0, 0), (1, 1)), mode="edge")
    lap_v = (edge[:, :, 2:] + edge[:, :, :-2] - 2.0 * cube).reshape(columns, 2 * LEVELS)
    return window + 0.2 * lap_h + 0.2 * lap_v + 1.5 * forcing - 0.05 * window


def per_device(
    spectrum, velocity, source_a, source_b, stokes_kernel, group_speed, column_map, land_mask
):
    bin_count = lax.axis_size("bin")
    device_count = lax.axis_size("band") * bin_count
    device = lax.axis_index("band") * bin_count + lax.axis_index("bin")
    cell_dev = spectrum.shape[0] // bin_count
    columns = velocity.shape[0]
    half = columns // 2
    total = columns * device_count
    bins = spectrum.shape[1] * bin_count

    cell_first = device * cell_dev
    ext_map = lax.dynamic_slice_in_dim(
        jnp.concatenate([column_map[-EXTRA:], column_map]), cell_first, cell_dev + EXTRA
    )
    ext_mask = lax.dynamic_slice_in_dim(
        jnp.concatenate([land_mask[-EXTRA:], land_mask]), cell_first, cell_dev + EXTRA
    ).astype(jnp.float32)
    local_map = ext_map[EXTRA:]
    local_mask = ext_mask[EXTRA:]
    cos_b, sin_b = bin_angles(bins)

    first = device * columns + half
    where = jnp.mod(local_map - first, total)
    onehot = (where[None, :] == jnp.arange(columns)[:, None]).astype(jnp.float32)
    counts = jnp.sum(onehot, axis=1)
    joint = (device == device_count - 1) if device_count > 1 else None

    upper = shifted(velocity[: half + 1], ALL, -1)
    window = jnp.concatenate([velocity[half:], upper[:half]], 0)
    below = velocity[half - 1 : half]
    above = upper[half:]

    own = jnp.concatenate([velocity, upper[:half]], 0)
    ext_where = jnp.mod(ext_map - device * columns, total)
    table = jnp.stack([own[:, 0], own[:, LEVELS]])
    current = jnp.take(table, ext_where, axis=1)

    body = lax.all_to_all(spectrum, "bin", split_axis=0, concat_axis=1, tiled=True)
    head = from_behind(body[-EXTRA:], ALL, 1)
    field = jnp.concatenate([head, body], 0)
    prev = jnp.zeros((1, bins), jnp.float32)
    mask = ext_mask
    for step in range(STEPS):
        moved = propagate(field, prev, current, group_speed, cos_b, sin_b, mask)
        increment, stokes = sources(
            moved.astype(jnp.bfloat16), mask, source_a, source_b, stokes_kernel
        )
        field = moved + increment.astype(jnp.float32)
        if step == 0:
            prev = field[EXTRA - 1 : EXTRA]
            field = field[EXTRA:]
            stokes = stokes[EXTRA:]
            mask = local_mask
        sums = jnp.dot(onehot, stokes, precision=lax.Precision.HIGHEST)
        forcing = sums / counts[:, None]
        if step > 0:
            below = shifted(window[-1:], ALL, 1)
            above = shifted(window[:1], ALL, -1)
        window = ocean_step(window, below, above, forcing, joint)
        if step + 1 < STEPS:
            table = jnp.stack([window[:, 0], window[:, LEVELS]])
            current = jnp.take(table, where, axis=1)
    velocity_out = jnp.concatenate([shifted(window[half:], ALL, 1), window[:half]], 0)
    spectrum_out = lax.all_to_all(field, "bin", split_axis=1, concat_axis=0, tiled=True)
    return (spectrum_out, velocity_out)


def solution(mesh):
    in_specs = (P("band", "bin"), P(ALL, None), P(), P(), P(), P(), P(), P())
    out_specs = (P("band", "bin"), P(ALL, None))
    return jax.shard_map(
        per_device, mesh=mesh, in_specs=in_specs, out_specs=out_specs, check_vma=False
    )
```

```python
import math

import jax
import jax.numpy as jnp
from jax import lax
from jax.sharding import PartitionSpec as P

NDIR = 36
LEVELS = 64
STEPS = 2
ALL = ("band", "bin")
EXTRA = 8


def shifted(block, axis, distance):
    devices = range(lax.axis_size(axis))
    route = [((i - distance) % len(devices), i) for i in devices]
    return lax.ppermute(block, axis, route)


def from_behind(shard, axis, by):
    peers = lax.axis_size(axis)
    pairs = [(i, i + by) for i in range(peers) if 0 <= i + by < peers]
    return lax.ppermute(shard, axis, pairs)


def bin_angles(count):
    index = jnp.arange(count)
    angle = 2.0 * math.pi / NDIR * (index % NDIR).astype(jnp.float32)
    return (jnp.cos(angle), jnp.sin(angle))


def propagate(field, prev, current, speed_bins, cos_b, sin_b, mask_cells):
    speed = speed_bins[None, :] + 0.25 * (
        jnp.tanh(current[0])[:, None] * cos_b[None, :]
        + jnp.tanh(current[1])[:, None] * sin_b[None, :]
    )
    behind = jnp.concatenate([prev, field[:-1]], 0)
    return mask_cells[:, None] * (field - speed * (field - behind))


def sources(rounded, mask_cells, source_a, source_b, stokes_kernel):
    gain = jnp.dot(rounded, source_a, preferred_element_type=jnp.float32)
    other = jnp.dot(rounded, source_b, preferred_element_type=jnp.float32)
    increment = (0.1 * mask_cells[:, None] * (gain + 0.5 * gain * other)).astype(jnp.bfloat16)
    stokes = jnp.dot(rounded, stokes_kernel, preferred_element_type=jnp.float32)
    return (increment, stokes)


def ocean_step(window, below, above, forcing, joint):
    columns = window.shape[0]
    padded = jnp.concatenate([below, window, above], 0)
    up = padded[2:]
    down = padded[:-2]
    if joint is not None:
        row = jnp.arange(columns)[:, None]
        up = jnp.where(joint & (row == columns // 2 - 1), 0.0, up)
        down = jnp.where(joint & (row == columns // 2), 0.0, down)
    lap_h = up + down - 2.0 * window
    cube = window.reshape(columns, 2, LEVELS)
    edge = jnp.pad(cube, ((0, 0), (0, 0), (1, 1)), mode="edge")
    lap_v = (edge[:, :, 2:] + edge[:, :, :-2] - 2.0 * cube).reshape(columns, 2 * LEVELS)
    return window + 0.2 * lap_h + 0.2 * lap_v + 1.5 * forcing - 0.05 * window


def ocean_rows(padded, forcing):
    columns = padded.shape[0] - 2
    window = padded[1:-1]
    lap_h = padded[2:] + padded[:-2] - 2.0 * window
    cube = window.reshape(columns, 2, LEVELS)
    edge = jnp.pad(cube, ((0, 0), (0, 0), (1, 1)), mode="edge")
    lap_v = (edge[:, :, 2:] + edge[:, :, :-2] - 2.0 * cube).reshape(columns, 2 * LEVELS)
    return window + 0.2 * lap_h + 0.2 * lap_v + 1.5 * forcing - 0.05 * window


def per_device(
    spectrum, velocity, source_a, source_b, stokes_kernel, group_speed, column_map, land_mask
):
    bin_count = lax.axis_size("bin")
    device_count = lax.axis_size("band") * bin_count
    device = lax.axis_index("band") * bin_count + lax.axis_index("bin")
    cell_dev = spectrum.shape[0] // bin_count
    columns = velocity.shape[0]
    half = columns // 2
    total = columns * device_count
    bins = spectrum.shape[1] * bin_count

    cell_first = device * cell_dev
    ext_map = lax.dynamic_slice_in_dim(
        jnp.concatenate([column_map[-EXTRA:], column_map]), cell_first, cell_dev + EXTRA
    )
    ext_mask = lax.dynamic_slice_in_dim(
        jnp.concatenate([land_mask[-EXTRA:], land_mask]), cell_first, cell_dev + EXTRA
    ).astype(jnp.float32)
    local_map = ext_map[EXTRA:]
    local_mask = ext_mask[EXTRA:]
    cos_b, sin_b = bin_angles(bins)

    first = device * columns + half
    where = jnp.mod(local_map - first, total)
    onehot = (where[None, :] == jnp.arange(columns)[:, None]).astype(jnp.float32)
    counts = jnp.sum(onehot, axis=1)
    joint = (device == device_count - 1) if device_count > 1 else None

    upper = shifted(velocity[: half + 1], ALL, -1)
    window = jnp.concatenate([velocity[half:], upper[:half]], 0)
    below = velocity[half - 1 : half]
    above = upper[half:]

    own = jnp.concatenate([velocity, upper[:half]], 0)
    ext_where = jnp.mod(ext_map - device * columns, total)
    table = jnp.stack([own[:, 0], own[:, LEVELS]])
    current = jnp.take(table, ext_where, axis=1)

    body = lax.all_to_all(spectrum, "bin", split_axis=0, concat_axis=1, tiled=True)
    head = from_behind(body[-EXTRA:], ALL, 1)
    field = jnp.concatenate([head, body], 0)
    prev = jnp.zeros((1, bins), jnp.float32)
    mask = ext_mask
    for step in range(STEPS):
        moved = propagate(field, prev, current, group_speed, cos_b, sin_b, mask)
        increment, stokes = sources(
            moved.astype(jnp.bfloat16), mask, source_a, source_b, stokes_kernel
        )
        field = moved + increment.astype(jnp.float32)
        if step == 0:
            prev = field[EXTRA - 1 : EXTRA]
            field = field[EXTRA:]
            stokes = stokes[EXTRA:]
            mask = local_mask
        sums = jnp.dot(onehot, stokes, precision=lax.Precision.HIGHEST)
        forcing = sums / counts[:, None]
        if step + 1 < STEPS:
            if step > 0:
                below = edge[-1:]
                above = shifted(window[:1], ALL, -1)
            window = ocean_step(window, below, above, forcing, joint)
            edge = shifted(window[half - 1 :], ALL, 1)
            table = jnp.stack([window[:, 0], window[:, LEVELS]])
            current = jnp.take(table, where, axis=1)
        else:
            low_forcing = shifted(forcing[half:], ALL, 1)
            padded = jnp.concatenate([edge, window[: half + 1]], 0)
            if device_count > 1:
                row = jnp.arange(padded.shape[0])[:, None]
                outside = ((device == 0) & (row == 0)) | (joint & (row == padded.shape[0] - 1))
                padded = jnp.where(outside, 0.0, padded)
            velocity_out = ocean_rows(padded, jnp.concatenate([low_forcing, forcing[:half]], 0))
    spectrum_out = lax.all_to_all(field, "bin", split_axis=1, concat_axis=0, tiled=True)
    return (spectrum_out, velocity_out)


def solution(mesh):
    in_specs = (P("band", "bin"), P(ALL, None), P(), P(), P(), P(), P(), P())
    out_specs = (P("band", "bin"), P(ALL, None))
    return jax.shard_map(
        per_device, mesh=mesh, in_specs=in_specs, out_specs=out_specs, check_vma=False
    )
```

```python
import math

import jax
import jax.numpy as jnp
from jax import lax
from jax.sharding import PartitionSpec as P


NDIR = 36
LEVELS = 64
STEPS = 2
ALL = ("band", "bin")
EXTRA = 8


def shifted(block, axis, distance):
    devices = range(lax.axis_size(axis))
    route = [((i - distance) % len(devices), i) for i in devices]
    return lax.ppermute(block, axis, route)


def from_behind(shard, axis, by):
    peers = lax.axis_size(axis)
    pairs = [(i, i + by) for i in range(peers) if 0 <= i + by < peers]
    return lax.ppermute(shard, axis, pairs)


def bin_angles(count):
    index = jnp.arange(count)
    angle = 2.0 * math.pi / NDIR * (index % NDIR).astype(jnp.float32)
    return (jnp.cos(angle), jnp.sin(angle))


def propagate(field, prev, current, speed_bins, cos_b, sin_b, mask_cells):
    speed = speed_bins[None, :] + 0.25 * (
        jnp.tanh(current[0])[:, None] * cos_b[None, :]
        + jnp.tanh(current[1])[:, None] * sin_b[None, :]
    )
    behind = jnp.concatenate([prev, field[:-1]], 0)
    return mask_cells[:, None] * (field - speed * (field - behind))


def sources(rounded, mask_cells, source_a, source_b, stokes_kernel):
    gain = jnp.dot(rounded, source_a, preferred_element_type=jnp.float32)
    other = jnp.dot(rounded, source_b, preferred_element_type=jnp.float32)
    increment = (0.1 * mask_cells[:, None] * (gain + 0.5 * gain * other)).astype(jnp.bfloat16)
    stokes = jnp.dot(rounded, stokes_kernel, preferred_element_type=jnp.float32)
    return (increment, stokes)


def ocean_step(window, below, above, forcing, joint):
    columns = window.shape[0]
    padded = jnp.concatenate([below, window, above], 0)
    up = padded[2:]
    down = padded[:-2]
    if joint is not None:
        row = jnp.arange(columns)[:, None]
        up = jnp.where(joint & (row == columns // 2 - 1), 0.0, up)
        down = jnp.where(joint & (row == columns // 2), 0.0, down)
    lap_h = up + down - 2.0 * window
    cube = window.reshape(columns, 2, LEVELS)
    edge = jnp.pad(cube, ((0, 0), (0, 0), (1, 1)), mode="edge")
    lap_v = (edge[:, :, 2:] + edge[:, :, :-2] - 2.0 * cube).reshape(columns, 2 * LEVELS)
    return window + 0.2 * lap_h + 0.2 * lap_v + 1.5 * forcing - 0.05 * window


def ocean_rows(padded, forcing):
    columns = padded.shape[0] - 2
    window = padded[1:-1]
    lap_h = padded[2:] + padded[:-2] - 2.0 * window
    cube = window.reshape(columns, 2, LEVELS)
    edge = jnp.pad(cube, ((0, 0), (0, 0), (1, 1)), mode="edge")
    lap_v = (edge[:, :, 2:] + edge[:, :, :-2] - 2.0 * cube).reshape(columns, 2 * LEVELS)
    return window + 0.2 * lap_h + 0.2 * lap_v + 1.5 * forcing - 0.05 * window


def steps(
    spectrum, velocity, source_a, source_b, stokes_kernel, group_speed, column_map, land_mask
):
    bin_count = lax.axis_size("bin")
    device_count = lax.axis_size("band") * bin_count
    device = lax.axis_index("band") * bin_count + lax.axis_index("bin")
    cell_dev = spectrum.shape[0] // bin_count
    columns = velocity.shape[0]
    half = columns // 2
    total = columns * device_count
    bins = spectrum.shape[1] * bin_count

    cell_first = device * cell_dev
    ext_map = lax.dynamic_slice_in_dim(
        jnp.concatenate([column_map[-EXTRA:], column_map]), cell_first, cell_dev + EXTRA
    )
    ext_mask = lax.dynamic_slice_in_dim(
        jnp.concatenate([land_mask[-EXTRA:], land_mask]), cell_first, cell_dev + EXTRA
    ).astype(jnp.float32)
    local_map = ext_map[EXTRA:]
    local_mask = ext_mask[EXTRA:]
    cos_b, sin_b = bin_angles(bins)

    first = device * columns + half
    where = jnp.mod(local_map - first, total)
    onehot = (where[None, :] == jnp.arange(columns)[:, None]).astype(jnp.float32)
    counts = jnp.sum(onehot, axis=1)
    joint = (device == device_count - 1) if device_count > 1 else None

    upper = shifted(velocity[: half + 1], ALL, -1)
    window = jnp.concatenate([velocity[half:], upper[:half]], 0)
    below = velocity[half - 1 : half]
    above = upper[half:]

    own = jnp.concatenate([velocity, upper[:half]], 0)
    ext_where = jnp.mod(ext_map - device * columns, total)
    table = jnp.stack([own[:, 0], own[:, LEVELS]])
    current = jnp.take(table, ext_where, axis=1)

    body = lax.all_to_all(spectrum, "bin", split_axis=0, concat_axis=1, tiled=True)
    head = from_behind(body[-EXTRA:], ALL, 1)
    field = jnp.concatenate([head, body], 0)
    prev = jnp.zeros((1, bins), jnp.float32)
    mask = ext_mask
    for step in range(STEPS):
        moved = propagate(field, prev, current, group_speed, cos_b, sin_b, mask)
        increment, stokes = sources(
            moved.astype(jnp.bfloat16), mask, source_a, source_b, stokes_kernel
        )
        field = moved + increment.astype(jnp.float32)
        if step == 0:
            prev = field[EXTRA - 1 : EXTRA]
            field = field[EXTRA:]
            stokes = stokes[EXTRA:]
            mask = local_mask
        sums = jnp.dot(onehot, stokes, precision=lax.Precision.HIGHEST)
        forcing = sums / counts[:, None]
        if step + 1 < STEPS:
            if step > 0:
                below = edge[-1:]
                above = shifted(window[:1], ALL, -1)
            window = ocean_step(window, below, above, forcing, joint)
            edge = shifted(window[half - 1 :], ALL, 1)
            table = jnp.stack([window[:, 0], window[:, LEVELS]])
            current = jnp.take(table, where, axis=1)
        else:
            low_forcing = shifted(forcing[half:], ALL, 1)
            padded = jnp.concatenate([edge, window[: half + 1]], 0)
            if device_count > 1:
                row = jnp.arange(padded.shape[0])[:, None]
                outside = ((device == 0) & (row == 0)) | (joint & (row == padded.shape[0] - 1))
                padded = jnp.where(outside, 0.0, padded)
            velocity_out = ocean_rows(padded, jnp.concatenate([low_forcing, forcing[:half]], 0))
    spectrum_out = lax.all_to_all(field, "bin", split_axis=1, concat_axis=0, tiled=True)
    return (spectrum_out, velocity_out)


def solution(mesh):
    in_specs = (P("band", "bin"), P(ALL, None), P(), P(), P(), P(), P(), P())
    out_specs = (P("band", "bin"), P(ALL, None))
    return jax.shard_map(steps, mesh=mesh, in_specs=in_specs, out_specs=out_specs, check_vma=False)
```

```python
import math

import jax
import jax.numpy as jnp
from jax import lax
from jax.sharding import PartitionSpec as P

NDIR = 36
LEVELS = 64
STEPS = 2
ALL = ("band", "bin")
EXTRA = 8


def shifted(block, axis, distance):
    devices = range(lax.axis_size(axis))
    route = [((i - distance) % len(devices), i) for i in devices]
    return lax.ppermute(block, axis, route)


def from_behind(shard, axis, by):
    peers = lax.axis_size(axis)
    pairs = [(i, i + by) for i in range(peers) if 0 <= i + by < peers]
    return lax.ppermute(shard, axis, pairs)


def bin_angles(count):
    index = jnp.arange(count)
    angle = 2.0 * math.pi / NDIR * (index % NDIR).astype(jnp.float32)
    return (jnp.cos(angle), jnp.sin(angle))


def propagate(field, prev, current, speed_bins, cos_b, sin_b, mask_cells):
    speed = speed_bins[None, :] + 0.25 * (
        jnp.tanh(current[0])[:, None] * cos_b[None, :]
        + jnp.tanh(current[1])[:, None] * sin_b[None, :]
    )
    behind = jnp.concatenate([prev, field[:-1]], 0)
    return mask_cells[:, None] * (field - speed * (field - behind))


def sources(rounded, mask_cells, source_a, source_b, stokes_kernel):
    gain = jnp.dot(rounded, source_a, preferred_element_type=jnp.float32)
    other = jnp.dot(rounded, source_b, preferred_element_type=jnp.float32)
    increment = (0.1 * mask_cells[:, None] * (gain + 0.5 * gain * other)).astype(jnp.bfloat16)
    stokes = jnp.dot(rounded, stokes_kernel, preferred_element_type=jnp.float32)
    return (increment, stokes)


def ocean_step(window, below, above, forcing, joint):
    columns = window.shape[0]
    padded = jnp.concatenate([below, window, above], 0)
    up = padded[2:]
    down = padded[:-2]
    if joint is not None:
        row = jnp.arange(columns)[:, None]
        up = jnp.where(joint & (row == columns // 2 - 1), 0.0, up)
        down = jnp.where(joint & (row == columns // 2), 0.0, down)
    lap_h = up + down - 2.0 * window
    cube = window.reshape(columns, 2, LEVELS)
    edge = jnp.pad(cube, ((0, 0), (0, 0), (1, 1)), mode="edge")
    lap_v = (edge[:, :, 2:] + edge[:, :, :-2] - 2.0 * cube).reshape(columns, 2 * LEVELS)
    return window + 0.2 * lap_h + 0.2 * lap_v + 1.5 * forcing - 0.05 * window


def ocean_rows(padded, forcing):
    columns = padded.shape[0] - 2
    window = padded[1:-1]
    lap_h = padded[2:] + padded[:-2] - 2.0 * window
    cube = window.reshape(columns, 2, LEVELS)
    edge = jnp.pad(cube, ((0, 0), (0, 0), (1, 1)), mode="edge")
    lap_v = (edge[:, :, 2:] + edge[:, :, :-2] - 2.0 * cube).reshape(columns, 2 * LEVELS)
    return window + 0.2 * lap_h + 0.2 * lap_v + 1.5 * forcing - 0.05 * window


def per_device(
    spectrum, velocity, source_a, source_b, stokes_kernel, group_speed, column_map, land_mask
):
    bin_count = lax.axis_size("bin")
    device_count = lax.axis_size("band") * bin_count
    device = lax.axis_index("band") * bin_count + lax.axis_index("bin")
    cell_dev = spectrum.shape[0] // bin_count
    columns = velocity.shape[0]
    half = columns // 2
    total = columns * device_count
    bins = spectrum.shape[1] * bin_count

    cell_first = device * cell_dev
    ext_map = lax.dynamic_slice_in_dim(
        jnp.concatenate([column_map[-EXTRA:], column_map]), cell_first, cell_dev + EXTRA
    )
    ext_mask = lax.dynamic_slice_in_dim(
        jnp.concatenate([land_mask[-EXTRA:], land_mask]), cell_first, cell_dev + EXTRA
    ).astype(jnp.float32)
    local_map = ext_map[EXTRA:]
    local_mask = ext_mask[EXTRA:]
    cos_b, sin_b = bin_angles(bins)

    first = device * columns + half
    where = jnp.mod(local_map - first, total)
    onehot = (where[None, :] == jnp.arange(columns)[:, None]).astype(jnp.float32)
    counts = jnp.sum(onehot, axis=1)
    joint = (device == device_count - 1) if device_count > 1 else None

    upper = shifted(velocity[: half + 1], ALL, -1)
    window = jnp.concatenate([velocity[half:], upper[:half]], 0)
    below = velocity[half - 1 : half]
    above = upper[half:]

    own = jnp.concatenate([velocity, upper[:half]], 0)
    ext_where = jnp.mod(ext_map - device * columns, total)
    table = jnp.stack([own[:, 0], own[:, LEVELS]])
    current = jnp.take(table, ext_where, axis=1)

    body = lax.all_to_all(spectrum, "bin", split_axis=0, concat_axis=1, tiled=True)
    head = from_behind(body[-EXTRA:], ALL, 1)
    head_current = current[:, :EXTRA]
    current = current[:, EXTRA:]
    head_mask = ext_mask[:EXTRA]
    head_moved = propagate(
        head, jnp.zeros((1, bins), jnp.float32), head_current, group_speed, cos_b, sin_b, head_mask
    )
    head_increment, _ = sources(
        head_moved.astype(jnp.bfloat16), head_mask, source_a, source_b, stokes_kernel
    )
    later_prev = (head_moved + head_increment.astype(jnp.float32))[-1:]
    field = body
    prev = head[-1:]
    for step in range(STEPS):
        moved = propagate(field, prev, current, group_speed, cos_b, sin_b, local_mask)
        increment, stokes = sources(
            moved.astype(jnp.bfloat16), local_mask, source_a, source_b, stokes_kernel
        )
        field = moved + increment.astype(jnp.float32)
        prev = later_prev
        sums = jnp.dot(onehot, stokes, precision=lax.Precision.HIGHEST)
        forcing = sums / counts[:, None]
        if step + 1 < STEPS:
            if step > 0:
                below = edge[-1:]
                above = shifted(window[:1], ALL, -1)
            window = ocean_step(window, below, above, forcing, joint)
            edge = shifted(window[half - 1 :], ALL, 1)
            table = jnp.stack([window[:, 0], window[:, LEVELS]])
            current = jnp.take(table, where, axis=1)
        else:
            low_forcing = shifted(forcing[half:], ALL, 1)
            padded = jnp.concatenate([edge, window[: half + 1]], 0)
            if device_count > 1:
                row = jnp.arange(padded.shape[0])[:, None]
                outside = ((device == 0) & (row == 0)) | (joint & (row == padded.shape[0] - 1))
                padded = jnp.where(outside, 0.0, padded)
            velocity_out = ocean_rows(padded, jnp.concatenate([low_forcing, forcing[:half]], 0))
    spectrum_out = lax.all_to_all(field, "bin", split_axis=1, concat_axis=0, tiled=True)
    return (spectrum_out, velocity_out)


def solution(mesh):
    in_specs = (P("band", "bin"), P(ALL, None), P(), P(), P(), P(), P(), P())
    out_specs = (P("band", "bin"), P(ALL, None))
    return jax.shard_map(
        per_device, mesh=mesh, in_specs=in_specs, out_specs=out_specs, check_vma=False
    )
```

```python
import math

import jax
import jax.numpy as jnp
from jax import lax
from jax.experimental.layout import Layout, with_layout_constraint
from jax.sharding import PartitionSpec as P

NDIR = 36
LEVELS = 64
STEPS = 2
ALL = ("band", "bin")
EXTRA = 8


def shifted(block, axis, distance):
    devices = range(lax.axis_size(axis))
    route = [((i - distance) % len(devices), i) for i in devices]
    return lax.ppermute(block, axis, route)


def from_behind(shard, axis, by):
    peers = lax.axis_size(axis)
    pairs = [(i, i + by) for i in range(peers) if 0 <= i + by < peers]
    return lax.ppermute(shard, axis, pairs)


def bin_angles(count):
    index = jnp.arange(count)
    angle = 2.0 * math.pi / NDIR * (index % NDIR).astype(jnp.float32)
    return (jnp.cos(angle), jnp.sin(angle))


def propagate(field, prev, current, speed_bins, cos_b, sin_b, mask_cells):
    speed = speed_bins[None, :] + 0.25 * (
        jnp.tanh(current[0])[:, None] * cos_b[None, :]
        + jnp.tanh(current[1])[:, None] * sin_b[None, :]
    )
    behind = jnp.concatenate([prev, field[:-1]], 0)
    return mask_cells[:, None] * (field - speed * (field - behind))


def sources(rounded, mask_cells, source_a, source_b, stokes_kernel):
    gain = jnp.dot(rounded, source_a, preferred_element_type=jnp.float32)
    other = jnp.dot(rounded, source_b, preferred_element_type=jnp.float32)
    increment = (0.1 * mask_cells[:, None] * (gain + 0.5 * gain * other)).astype(jnp.bfloat16)
    stokes = jnp.dot(rounded, stokes_kernel, preferred_element_type=jnp.float32)
    return (increment, stokes)


def ocean_step(window, below, above, forcing, joint):
    columns = window.shape[0]
    padded = jnp.concatenate([below, window, above], 0)
    up = padded[2:]
    down = padded[:-2]
    if joint is not None:
        row = jnp.arange(columns)[:, None]
        up = jnp.where(joint & (row == columns // 2 - 1), 0.0, up)
        down = jnp.where(joint & (row == columns // 2), 0.0, down)
    lap_h = up + down - 2.0 * window
    cube = window.reshape(columns, 2, LEVELS)
    edge = jnp.pad(cube, ((0, 0), (0, 0), (1, 1)), mode="edge")
    lap_v = (edge[:, :, 2:] + edge[:, :, :-2] - 2.0 * cube).reshape(columns, 2 * LEVELS)
    return window + 0.2 * lap_h + 0.2 * lap_v + 1.5 * forcing - 0.05 * window


def ocean_rows(padded, forcing):
    columns = padded.shape[0] - 2
    window = padded[1:-1]
    lap_h = padded[2:] + padded[:-2] - 2.0 * window
    cube = window.reshape(columns, 2, LEVELS)
    edge = jnp.pad(cube, ((0, 0), (0, 0), (1, 1)), mode="edge")
    lap_v = (edge[:, :, 2:] + edge[:, :, :-2] - 2.0 * cube).reshape(columns, 2 * LEVELS)
    return window + 0.2 * lap_h + 0.2 * lap_v + 1.5 * forcing - 0.05 * window


def per_device(
    spectrum, velocity, source_a, source_b, stokes_kernel, group_speed, column_map, land_mask
):
    bin_count = lax.axis_size("bin")
    device_count = lax.axis_size("band") * bin_count
    device = lax.axis_index("band") * bin_count + lax.axis_index("bin")
    cell_dev = spectrum.shape[0] // bin_count
    columns = velocity.shape[0]
    half = columns // 2
    total = columns * device_count
    bins = spectrum.shape[1] * bin_count

    cell_first = device * cell_dev
    ext_map = lax.dynamic_slice_in_dim(
        jnp.concatenate([column_map[-EXTRA:], column_map]), cell_first, cell_dev + EXTRA
    )
    ext_mask = lax.dynamic_slice_in_dim(
        jnp.concatenate([land_mask[-EXTRA:], land_mask]), cell_first, cell_dev + EXTRA
    ).astype(jnp.float32)
    local_map = ext_map[EXTRA:]
    local_mask = ext_mask[EXTRA:]
    cos_b, sin_b = bin_angles(bins)

    first = device * columns + half
    where = jnp.mod(local_map - first, total)
    onehot = (where[None, :] == jnp.arange(columns)[:, None]).astype(jnp.float32)
    counts = jnp.sum(onehot, axis=1)
    joint = (device == device_count - 1) if device_count > 1 else None

    upper = shifted(velocity[: half + 1], ALL, -1)
    window = jnp.concatenate([velocity[half:], upper[:half]], 0)
    below = velocity[half - 1 : half]
    above = upper[half:]

    own = jnp.concatenate([velocity, upper[:half]], 0)
    ext_where = jnp.mod(ext_map - device * columns, total)
    table = jnp.stack([own[:, 0], own[:, LEVELS]])
    current = jnp.take(table, ext_where, axis=1)

    body = lax.all_to_all(spectrum, "bin", split_axis=0, concat_axis=1, tiled=True)
    head = from_behind(body[-EXTRA:], ALL, 1)
    field = jnp.concatenate([head, body], 0)
    prev = jnp.zeros((1, bins), jnp.float32)
    mask = ext_mask
    for step in range(STEPS):
        moved = propagate(field, prev, current, group_speed, cos_b, sin_b, mask)
        increment, stokes = sources(
            moved.astype(jnp.bfloat16), mask, source_a, source_b, stokes_kernel
        )
        field = moved + increment.astype(jnp.float32)
        if step == 0:
            prev = field[EXTRA - 1 : EXTRA]
            field = field[EXTRA:]
            stokes = stokes[EXTRA:]
            mask = local_mask
        sums = jnp.dot(onehot, stokes, precision=lax.Precision.HIGHEST)
        forcing = sums / counts[:, None]
        if step + 1 < STEPS:
            if step > 0:
                below = edge[-1:]
                above = shifted(window[:1], ALL, -1)
            window = ocean_step(window, below, above, forcing, joint)
            edge = shifted(window[half - 1 :], ALL, 1)
            table = jnp.stack([window[:, 0], window[:, LEVELS]])
            current = jnp.take(table, where, axis=1)
        else:
            low_forcing = shifted(forcing[half:], ALL, 1)
            padded = jnp.concatenate([edge, window[: half + 1]], 0)
            if device_count > 1:
                row = jnp.arange(padded.shape[0])[:, None]
                outside = ((device == 0) & (row == 0)) | (joint & (row == padded.shape[0] - 1))
                padded = jnp.where(outside, 0.0, padded)
            velocity_out = ocean_rows(padded, jnp.concatenate([low_forcing, forcing[:half]], 0))
    field = with_layout_constraint(field, Layout(major_to_minor=(1, 0)))
    spectrum_out = lax.all_to_all(field, "bin", split_axis=1, concat_axis=0, tiled=True)
    return (spectrum_out, velocity_out)


def solution(mesh):
    in_specs = (P("band", "bin"), P(ALL, None), P(), P(), P(), P(), P(), P())
    out_specs = (P("band", "bin"), P(ALL, None))
    return jax.shard_map(
        per_device, mesh=mesh, in_specs=in_specs, out_specs=out_specs, check_vma=False
    )
```

```python
import math

import jax
import jax.numpy as jnp
from jax import lax
from jax.sharding import PartitionSpec as P

NDIR = 36
LEVELS = 64
STEPS = 2
ALL = ("band", "bin")
EXTRA = 8


def shifted(block, axis, distance):
    devices = range(lax.axis_size(axis))
    route = [((i - distance) % len(devices), i) for i in devices]
    return lax.ppermute(block, axis, route)


def from_behind(shard, axis, by):
    peers = lax.axis_size(axis)
    pairs = [(i, i + by) for i in range(peers) if 0 <= i + by < peers]
    return lax.ppermute(shard, axis, pairs)


def bin_angles(count):
    index = jnp.arange(count)
    angle = 2.0 * math.pi / NDIR * (index % NDIR).astype(jnp.float32)
    return (jnp.cos(angle), jnp.sin(angle))


def propagate(field, prev, current, speed_bins, cos_b, sin_b, mask_cells):
    speed = speed_bins[None, :] + 0.25 * (
        jnp.tanh(current[0])[:, None] * cos_b[None, :]
        + jnp.tanh(current[1])[:, None] * sin_b[None, :]
    )
    behind = jnp.concatenate([prev, field[:-1]], 0)
    return mask_cells[:, None] * (field - speed * (field - behind))


def sources(rounded, mask_cells, source_a, source_b, stokes_kernel):
    gain = jnp.dot(rounded, source_a, preferred_element_type=jnp.float32)
    other = jnp.dot(rounded, source_b, preferred_element_type=jnp.float32)
    increment = (0.1 * mask_cells[:, None] * (gain + 0.5 * gain * other)).astype(jnp.bfloat16)
    stokes = jnp.dot(rounded, stokes_kernel, preferred_element_type=jnp.float32)
    return (increment, stokes)


def ocean_step(window, below, above, forcing, joint):
    columns = window.shape[0]
    padded = jnp.concatenate([below, window, above], 0)
    up = padded[2:]
    down = padded[:-2]
    if joint is not None:
        row = jnp.arange(columns)[:, None]
        up = jnp.where(joint & (row == columns // 2 - 1), 0.0, up)
        down = jnp.where(joint & (row == columns // 2), 0.0, down)
    lap_h = up + down - 2.0 * window
    cube = window.reshape(columns, 2, LEVELS)
    edge = jnp.pad(cube, ((0, 0), (0, 0), (1, 1)), mode="edge")
    lap_v = (edge[:, :, 2:] + edge[:, :, :-2] - 2.0 * cube).reshape(columns, 2 * LEVELS)
    return window + 0.2 * lap_h + 0.2 * lap_v + 1.5 * forcing - 0.05 * window


def ocean_rows(padded, forcing):
    columns = padded.shape[0] - 2
    window = padded[1:-1]
    lap_h = padded[2:] + padded[:-2] - 2.0 * window
    cube = window.reshape(columns, 2, LEVELS)
    edge = jnp.pad(cube, ((0, 0), (0, 0), (1, 1)), mode="edge")
    lap_v = (edge[:, :, 2:] + edge[:, :, :-2] - 2.0 * cube).reshape(columns, 2 * LEVELS)
    return window + 0.2 * lap_h + 0.2 * lap_v + 1.5 * forcing - 0.05 * window


def per_device(
    spectrum, velocity, source_a, source_b, stokes_kernel, group_speed, column_map, land_mask
):
    bin_count = lax.axis_size("bin")
    device_count = lax.axis_size("band") * bin_count
    device = lax.axis_index("band") * bin_count + lax.axis_index("bin")
    cell_dev = spectrum.shape[0] // bin_count
    columns = velocity.shape[0]
    half = columns // 2
    total = columns * device_count
    bins = spectrum.shape[1] * bin_count

    cell_first = device * cell_dev
    ext_map = lax.dynamic_slice_in_dim(
        jnp.concatenate([column_map[-EXTRA:], column_map]), cell_first, cell_dev + EXTRA
    )
    ext_mask = lax.dynamic_slice_in_dim(
        jnp.concatenate([land_mask[-EXTRA:], land_mask]), cell_first, cell_dev + EXTRA
    ).astype(jnp.float32)
    local_map = ext_map[EXTRA:]
    local_mask = ext_mask[EXTRA:]
    cos_b, sin_b = bin_angles(bins)

    first = device * columns + half
    where = jnp.mod(local_map - first, total)
    onehot = (where[None, :] == jnp.arange(columns)[:, None]).astype(jnp.float32)
    counts = jnp.sum(onehot, axis=1)
    joint = (device == device_count - 1) if device_count > 1 else None

    upper = shifted(velocity[: half + 1], ALL, -1)
    window = jnp.concatenate([velocity[half:], upper[:half]], 0)
    below = velocity[half - 1 : half]
    above = upper[half:]

    own = jnp.concatenate([velocity, upper[:half]], 0)
    ext_where = jnp.mod(ext_map - device * columns, total)
    table = jnp.stack([own[:, 0], own[:, LEVELS]])
    current = jnp.take(table, ext_where, axis=1)

    field = lax.all_to_all(spectrum, "bin", split_axis=0, concat_axis=1, tiled=True)
    current = current[:, EXTRA:]
    for step in range(STEPS):
        prev = from_behind(field[-1:], ALL, 1)
        moved = propagate(field, prev, current, group_speed, cos_b, sin_b, local_mask)
        increment, stokes = sources(
            moved.astype(jnp.bfloat16), local_mask, source_a, source_b, stokes_kernel
        )
        field = moved + increment.astype(jnp.float32)
        sums = jnp.dot(onehot, stokes, precision=lax.Precision.HIGHEST)
        forcing = sums / counts[:, None]
        if step + 1 < STEPS:
            if step > 0:
                below = edge[-1:]
                above = shifted(window[:1], ALL, -1)
            window = ocean_step(window, below, above, forcing, joint)
            edge = shifted(window[half - 1 :], ALL, 1)
            table = jnp.stack([window[:, 0], window[:, LEVELS]])
            current = jnp.take(table, where, axis=1)
        else:
            low_forcing = shifted(forcing[half:], ALL, 1)
            padded = jnp.concatenate([edge, window[: half + 1]], 0)
            if device_count > 1:
                row = jnp.arange(padded.shape[0])[:, None]
                outside = ((device == 0) & (row == 0)) | (joint & (row == padded.shape[0] - 1))
                padded = jnp.where(outside, 0.0, padded)
            velocity_out = ocean_rows(padded, jnp.concatenate([low_forcing, forcing[:half]], 0))
    spectrum_out = lax.all_to_all(field, "bin", split_axis=1, concat_axis=0, tiled=True)
    return (spectrum_out, velocity_out)


def solution(mesh):
    in_specs = (P("band", "bin"), P(ALL, None), P(), P(), P(), P(), P(), P())
    out_specs = (P("band", "bin"), P(ALL, None))
    return jax.shard_map(
        per_device, mesh=mesh, in_specs=in_specs, out_specs=out_specs, check_vma=False
    )
```

```python
import math

import jax
import jax.numpy as jnp
from jax import lax
from jax.sharding import PartitionSpec as P

NDIR = 36
LEVELS = 64
STEPS = 2
ALL = ("band", "bin")
EXTRA = 16


def shifted(block, axis, distance):
    devices = range(lax.axis_size(axis))
    route = [((i - distance) % len(devices), i) for i in devices]
    return lax.ppermute(block, axis, route)


def from_behind(shard, axis, by):
    peers = lax.axis_size(axis)
    pairs = [(i, i + by) for i in range(peers) if 0 <= i + by < peers]
    return lax.ppermute(shard, axis, pairs)


def bin_angles(count):
    index = jnp.arange(count)
    angle = 2.0 * math.pi / NDIR * (index % NDIR).astype(jnp.float32)
    return (jnp.cos(angle), jnp.sin(angle))


def propagate(field, prev, current, speed_bins, cos_b, sin_b, mask_cells):
    speed = speed_bins[None, :] + 0.25 * (
        jnp.tanh(current[0])[:, None] * cos_b[None, :]
        + jnp.tanh(current[1])[:, None] * sin_b[None, :]
    )
    behind = jnp.concatenate([prev, field[:-1]], 0)
    return mask_cells[:, None] * (field - speed * (field - behind))


def sources(rounded, mask_cells, source_a, source_b, stokes_kernel):
    gain = jnp.dot(rounded, source_a, preferred_element_type=jnp.float32)
    other = jnp.dot(rounded, source_b, preferred_element_type=jnp.float32)
    increment = (0.1 * mask_cells[:, None] * (gain + 0.5 * gain * other)).astype(jnp.bfloat16)
    stokes = jnp.dot(rounded, stokes_kernel, preferred_element_type=jnp.float32)
    return (increment, stokes)


def ocean_step(window, below, above, forcing, joint):
    columns = window.shape[0]
    padded = jnp.concatenate([below, window, above], 0)
    up = padded[2:]
    down = padded[:-2]
    if joint is not None:
        row = jnp.arange(columns)[:, None]
        up = jnp.where(joint & (row == columns // 2 - 1), 0.0, up)
        down = jnp.where(joint & (row == columns // 2), 0.0, down)
    lap_h = up + down - 2.0 * window
    cube = window.reshape(columns, 2, LEVELS)
    edge = jnp.pad(cube, ((0, 0), (0, 0), (1, 1)), mode="edge")
    lap_v = (edge[:, :, 2:] + edge[:, :, :-2] - 2.0 * cube).reshape(columns, 2 * LEVELS)
    return window + 0.2 * lap_h + 0.2 * lap_v + 1.5 * forcing - 0.05 * window


def ocean_rows(padded, forcing):
    columns = padded.shape[0] - 2
    window = padded[1:-1]
    lap_h = padded[2:] + padded[:-2] - 2.0 * window
    cube = window.reshape(columns, 2, LEVELS)
    edge = jnp.pad(cube, ((0, 0), (0, 0), (1, 1)), mode="edge")
    lap_v = (edge[:, :, 2:] + edge[:, :, :-2] - 2.0 * cube).reshape(columns, 2 * LEVELS)
    return window + 0.2 * lap_h + 0.2 * lap_v + 1.5 * forcing - 0.05 * window


def per_device(
    spectrum, velocity, source_a, source_b, stokes_kernel, group_speed, column_map, land_mask
):
    bin_count = lax.axis_size("bin")
    device_count = lax.axis_size("band") * bin_count
    device = lax.axis_index("band") * bin_count + lax.axis_index("bin")
    cell_dev = spectrum.shape[0] // bin_count
    columns = velocity.shape[0]
    half = columns // 2
    total = columns * device_count
    bins = spectrum.shape[1] * bin_count

    cell_first = device * cell_dev
    ext_map = lax.dynamic_slice_in_dim(
        jnp.concatenate([column_map[-EXTRA:], column_map]), cell_first, cell_dev + EXTRA
    )
    ext_mask = lax.dynamic_slice_in_dim(
        jnp.concatenate([land_mask[-EXTRA:], land_mask]), cell_first, cell_dev + EXTRA
    ).astype(jnp.float32)
    local_map = ext_map[EXTRA:]
    local_mask = ext_mask[EXTRA:]
    cos_b, sin_b = bin_angles(bins)

    first = device * columns + half
    where = jnp.mod(local_map - first, total)
    onehot = (where[None, :] == jnp.arange(columns)[:, None]).astype(jnp.float32)
    counts = jnp.sum(onehot, axis=1)
    joint = (device == device_count - 1) if device_count > 1 else None

    upper = shifted(velocity[: half + 1], ALL, -1)
    window = jnp.concatenate([velocity[half:], upper[:half]], 0)
    below = velocity[half - 1 : half]
    above = upper[half:]

    own = jnp.concatenate([velocity, upper[:half]], 0)
    ext_where = jnp.mod(ext_map - device * columns, total)
    table = jnp.stack([own[:, 0], own[:, LEVELS]])
    current = jnp.take(table, ext_where, axis=1)

    body = lax.all_to_all(spectrum, "bin", split_axis=0, concat_axis=1, tiled=True)
    head = from_behind(body[-EXTRA:], ALL, 1)
    field = jnp.concatenate([head, body], 0)
    prev = jnp.zeros((1, bins), jnp.float32)
    mask = ext_mask
    for step in range(STEPS):
        moved = propagate(field, prev, current, group_speed, cos_b, sin_b, mask)
        increment, stokes = sources(
            moved.astype(jnp.bfloat16), mask, source_a, source_b, stokes_kernel
        )
        field = moved + increment.astype(jnp.float32)
        if step == 0:
            prev = field[EXTRA - 1 : EXTRA]
            field = field[EXTRA:]
            stokes = stokes[EXTRA:]
            mask = local_mask
        sums = jnp.dot(onehot, stokes, precision=lax.Precision.HIGHEST)
        forcing = sums / counts[:, None]
        if step + 1 < STEPS:
            if step > 0:
                below = edge[-1:]
                above = shifted(window[:1], ALL, -1)
            window = ocean_step(window, below, above, forcing, joint)
            edge = shifted(window[half - 1 :], ALL, 1)
            table = jnp.stack([window[:, 0], window[:, LEVELS]])
            current = jnp.take(table, where, axis=1)
        else:
            low_forcing = shifted(forcing[half:], ALL, 1)
            padded = jnp.concatenate([edge, window[: half + 1]], 0)
            if device_count > 1:
                row = jnp.arange(padded.shape[0])[:, None]
                outside = ((device == 0) & (row == 0)) | (joint & (row == padded.shape[0] - 1))
                padded = jnp.where(outside, 0.0, padded)
            velocity_out = ocean_rows(padded, jnp.concatenate([low_forcing, forcing[:half]], 0))
    spectrum_out = lax.all_to_all(field, "bin", split_axis=1, concat_axis=0, tiled=True)
    return (spectrum_out, velocity_out)


def solution(mesh):
    in_specs = (P("band", "bin"), P(ALL, None), P(), P(), P(), P(), P(), P())
    out_specs = (P("band", "bin"), P(ALL, None))
    return jax.shard_map(
        per_device, mesh=mesh, in_specs=in_specs, out_specs=out_specs, check_vma=False
    )
```

```python
import math

import jax
import jax.numpy as jnp
from jax import lax
from jax.sharding import PartitionSpec as P

NDIR = 36
LEVELS = 64
STEPS = 2
ALL = ("band", "bin")
EXTRA = 8


def shifted(block, axis, distance):
    devices = range(lax.axis_size(axis))
    route = [((i - distance) % len(devices), i) for i in devices]
    return lax.ppermute(block, axis, route)


def from_behind(shard, axis, by):
    peers = lax.axis_size(axis)
    pairs = [(i, i + by) for i in range(peers) if 0 <= i + by < peers]
    return lax.ppermute(shard, axis, pairs)


def bin_angles(count):
    index = jnp.arange(count)
    angle = 2.0 * math.pi / NDIR * (index % NDIR).astype(jnp.float32)
    return (jnp.cos(angle), jnp.sin(angle))


def propagate(field, prev, current, speed_bins, cos_b, sin_b, mask_cells):
    speed = speed_bins[None, :] + 0.25 * (
        jnp.tanh(current[0])[:, None] * cos_b[None, :]
        + jnp.tanh(current[1])[:, None] * sin_b[None, :]
    )
    behind = jnp.concatenate([prev, field[:-1]], 0)
    return mask_cells[:, None] * (field - speed * (field - behind))


def sources(rounded, mask_cells, joined, source_b, stokes_kernel):
    both = jnp.dot(rounded, joined, preferred_element_type=jnp.float32)
    gain = both[:, : source_b.shape[1]]
    stokes = both[:, source_b.shape[1] :]
    other = jnp.dot(rounded, source_b, preferred_element_type=jnp.float32)
    increment = (0.1 * mask_cells[:, None] * (gain + 0.5 * gain * other)).astype(jnp.bfloat16)
    return (increment, stokes)


def ocean_step(window, below, above, forcing, joint):
    columns = window.shape[0]
    padded = jnp.concatenate([below, window, above], 0)
    up = padded[2:]
    down = padded[:-2]
    if joint is not None:
        row = jnp.arange(columns)[:, None]
        up = jnp.where(joint & (row == columns // 2 - 1), 0.0, up)
        down = jnp.where(joint & (row == columns // 2), 0.0, down)
    lap_h = up + down - 2.0 * window
    cube = window.reshape(columns, 2, LEVELS)
    edge = jnp.pad(cube, ((0, 0), (0, 0), (1, 1)), mode="edge")
    lap_v = (edge[:, :, 2:] + edge[:, :, :-2] - 2.0 * cube).reshape(columns, 2 * LEVELS)
    return window + 0.2 * lap_h + 0.2 * lap_v + 1.5 * forcing - 0.05 * window


def ocean_rows(padded, forcing):
    columns = padded.shape[0] - 2
    window = padded[1:-1]
    lap_h = padded[2:] + padded[:-2] - 2.0 * window
    cube = window.reshape(columns, 2, LEVELS)
    edge = jnp.pad(cube, ((0, 0), (0, 0), (1, 1)), mode="edge")
    lap_v = (edge[:, :, 2:] + edge[:, :, :-2] - 2.0 * cube).reshape(columns, 2 * LEVELS)
    return window + 0.2 * lap_h + 0.2 * lap_v + 1.5 * forcing - 0.05 * window


def per_device(
    spectrum, velocity, source_a, source_b, stokes_kernel, group_speed, column_map, land_mask
):
    bin_count = lax.axis_size("bin")
    device_count = lax.axis_size("band") * bin_count
    device = lax.axis_index("band") * bin_count + lax.axis_index("bin")
    cell_dev = spectrum.shape[0] // bin_count
    columns = velocity.shape[0]
    half = columns // 2
    total = columns * device_count
    bins = spectrum.shape[1] * bin_count

    cell_first = device * cell_dev
    ext_map = lax.dynamic_slice_in_dim(
        jnp.concatenate([column_map[-EXTRA:], column_map]), cell_first, cell_dev + EXTRA
    )
    ext_mask = lax.dynamic_slice_in_dim(
        jnp.concatenate([land_mask[-EXTRA:], land_mask]), cell_first, cell_dev + EXTRA
    ).astype(jnp.float32)
    local_map = ext_map[EXTRA:]
    local_mask = ext_mask[EXTRA:]
    cos_b, sin_b = bin_angles(bins)
    joined = jnp.concatenate([source_a, stokes_kernel], 1)

    first = device * columns + half
    where = jnp.mod(local_map - first, total)
    onehot = (where[None, :] == jnp.arange(columns)[:, None]).astype(jnp.float32)
    counts = jnp.sum(onehot, axis=1)
    joint = (device == device_count - 1) if device_count > 1 else None

    upper = shifted(velocity[: half + 1], ALL, -1)
    window = jnp.concatenate([velocity[half:], upper[:half]], 0)
    below = velocity[half - 1 : half]
    above = upper[half:]

    own = jnp.concatenate([velocity, upper[:half]], 0)
    ext_where = jnp.mod(ext_map - device * columns, total)
    table = jnp.stack([own[:, 0], own[:, LEVELS]])
    current = jnp.take(table, ext_where, axis=1)

    body = lax.all_to_all(spectrum, "bin", split_axis=0, concat_axis=1, tiled=True)
    head = from_behind(body[-EXTRA:], ALL, 1)
    field = jnp.concatenate([head, body], 0)
    prev = jnp.zeros((1, bins), jnp.float32)
    mask = ext_mask
    for step in range(STEPS):
        moved = propagate(field, prev, current, group_speed, cos_b, sin_b, mask)
        increment, stokes = sources(
            moved.astype(jnp.bfloat16), mask, joined, source_b, stokes_kernel
        )
        field = moved + increment.astype(jnp.float32)
        if step == 0:
            prev = field[EXTRA - 1 : EXTRA]
            field = field[EXTRA:]
            stokes = stokes[EXTRA:]
            mask = local_mask
        sums = jnp.dot(onehot, stokes, precision=lax.Precision.HIGHEST)
        forcing = sums / counts[:, None]
        if step + 1 < STEPS:
            if step > 0:
                below = edge[-1:]
                above = shifted(window[:1], ALL, -1)
            window = ocean_step(window, below, above, forcing, joint)
            edge = shifted(window[half - 1 :], ALL, 1)
            table = jnp.stack([window[:, 0], window[:, LEVELS]])
            current = jnp.take(table, where, axis=1)
        else:
            low_forcing = shifted(forcing[half:], ALL, 1)
            padded = jnp.concatenate([edge, window[: half + 1]], 0)
            if device_count > 1:
                row = jnp.arange(padded.shape[0])[:, None]
                outside = ((device == 0) & (row == 0)) | (joint & (row == padded.shape[0] - 1))
                padded = jnp.where(outside, 0.0, padded)
            velocity_out = ocean_rows(padded, jnp.concatenate([low_forcing, forcing[:half]], 0))
    spectrum_out = lax.all_to_all(field, "bin", split_axis=1, concat_axis=0, tiled=True)
    return (spectrum_out, velocity_out)


def solution(mesh):
    in_specs = (P("band", "bin"), P(ALL, None), P(), P(), P(), P(), P(), P())
    out_specs = (P("band", "bin"), P(ALL, None))
    return jax.shard_map(
        per_device, mesh=mesh, in_specs=in_specs, out_specs=out_specs, check_vma=False
    )
```
